512 devices in a mesh: path: 32 (over x, y, core), tensor: 16 (over z).
Axes of the slice: x: 4, y: 4, z: 16, core: 2. Of those that a mesh axis runs over, the one named last changes fastest.
Arguments:
- hidden_in: bfloat16 [12288, 2048], P(('path', 'tensor')), may hold values from -120 to 120
- teacher: bfloat16 [12288, 2048], P('path'), may hold values from -3 to 3
- params: bfloat16 [3, 3, 7168, 2048], P(None, None, ('tensor', 'path')), may hold values from -4 to 4
- momentum: float32 [3, 3, 7168, 2048], P(None, None, ('tensor', 'path')), may hold values from -3 to 3
- path_alive: int32 [32], replicated, may hold values from 0 to 1, as said below
- path_module: int32 [32], replicated, may hold values from 0 to 2, as said below
Outputs:
- new_params: bfloat16 [3, 3, 7168, 2048], P(None, None, ('tensor', 'path'))
- new_momentum: float32 [3, 3, 7168, 2048], P(None, None, ('tensor', 'path'))
The draws below stay inside these ranges and needn't reach their ends.
Inputs may be any that keep to these rules, and one draw needn't show every extreme that they name: `path_alive`: at least one path is dead. `path_module`: every one of the 3 modules is used by at least one path whose path_alive entry is 1.
All inputs are finite; a program needn't handle non-finite values.
Results may differ from the reference program's by a relative error of at most 0.0047.
Values may be sent and summed in bfloat16 or wider, within the bound.
No kernel may reach another device: no remote copies, remote signals or barrier semaphores. Data moves between devices by JAX's collectives and lax.ppermute only.
A program may use at most 64 MiB of HBM per device.

```python
import math
import jax
import jax.numpy as jnp
from jax import lax

D = 2048
FW = 7168
TOK = 384
MODS = 3
PATHS = 32


def draw_hidden_in(key, part):
    keys = jax.random.split(key, 3)
    row_count = PATHS * TOK
    row_scale = jnp.exp(jax.random.uniform(keys[0], (row_count, 1), jnp.float32, 0.0, math.log(10.0)))
    col_scale = jnp.exp(jax.random.uniform(keys[1], (1, D), jnp.float32, 0.0, math.log(3.0)))
    values = jnp.clip(jax.random.normal(keys[2], (row_count, D), jnp.float32), -4.0, 4.0) * row_scale * col_scale
    return values.astype(jnp.bfloat16)


def path_tables(key):
    base_key = jax.random.fold_in(key, 101)
    keys = jax.random.split(base_key, 4)
    levels = jax.random.randint(keys[0], (PATHS,), 1, 2 ** MODS)
    ranking = jnp.zeros((PATHS,), jnp.int32)
    for bit_pos in range(1, MODS):
        ranking = ranking + (levels >= 2 ** bit_pos).astype(jnp.int32)
    ordering = jax.random.permutation(keys[1], MODS).astype(jnp.int32)
    module = jnp.take(ordering, ranking)
    anchors = jax.random.permutation(keys[2], PATHS).astype(jnp.int32)
    chosen = anchors[:MODS]
    module = module.at[chosen].set(jnp.arange(MODS, dtype=jnp.int32))
    alive_flags = (jax.random.randint(keys[3], (PATHS,), 0, 4) > 0).astype(jnp.int32)
    alive_flags = alive_flags.at[chosen].set(1)
    alive_flags = alive_flags.at[anchors[MODS]].set(0)
    return (alive_flags, module.astype(jnp.int32))


def draw_path_alive(key, part):
    return path_tables(key)[0]


def draw_path_module(key, part):
    return path_tables(key)[1]


def block_scale(stream_key, dims, cuts, smallest, high):
    loudness = 1.0
    for dim, parts in cuts:
        draws = jax.random.uniform(jax.random.fold_in(jax.random.fold_in(stream_key, 6), dim), (parts,), jnp.float32, smallest / len(cuts), high / len(cuts))
        loudness = loudness * jnp.repeat(jnp.exp(draws), dims[dim] // parts).reshape((-1,) + (1,) * (len(dims) - 1 - dim))
    return loudness


def normal_values(key, extent, scale, reach, cuts=(), kind=jnp.bfloat16):
    loudness = block_scale(key, extent, cuts, -0.22, 0.18) if cuts else 1.0
    array = jax.random.normal(key, extent, jnp.float32) * scale * loudness
    return jnp.minimum(jnp.maximum(array, -reach), reach).astype(kind)


def setup_inputs(seed: int = 0) -> dict:
    arg_keys = jax.random.split(jax.random.key(seed), 7)
    hidden_in = draw_hidden_in(jax.random.fold_in(arg_keys[6], 71), 0)
    teacher = normal_values(arg_keys[1], (PATHS * TOK, D), 0.5, 3.0, ((0, 32),))
    params = normal_values(arg_keys[2], (MODS, 3, FW, D), 1.0, 4.0, ((2, 512),))
    momentum = normal_values(arg_keys[3], (MODS, 3, FW, D), 0.5, 3.0, ((2, 512),), jnp.float32)
    path_alive = draw_path_alive(jax.random.fold_in(arg_keys[6], 71), 0)
    path_module = draw_path_module(jax.random.fold_in(arg_keys[6], 71), 0)
    return {"hidden_in": hidden_in, "teacher": teacher, "params": params, "momentum": momentum, "path_alive": path_alive, "path_module": path_module}


def path_delta(rows_in, target, weights):
    mean_sq = lax.optimization_barrier(jnp.mean(jnp.square(rows_in.astype(jnp.float32)), axis=1, keepdims=True))
    normed = (rows_in.astype(jnp.float32) * lax.rsqrt(mean_sq + 1e-05)).astype(jnp.bfloat16)
    gate_pre = jnp.dot(normed, weights[0].T, preferred_element_type=jnp.float32) / math.sqrt(D)
    up_proj = jnp.dot(normed, weights[1].T, preferred_element_type=jnp.float32) / math.sqrt(D)
    sigmoid_gate = jax.nn.sigmoid(gate_pre)
    activated = gate_pre * sigmoid_gate
    hidden = (activated * up_proj).astype(jnp.bfloat16)
    output = jnp.dot(hidden, weights[2], preferred_element_type=jnp.float32) / math.sqrt(FW)
    cotangent = (4.0 * (output - target.astype(jnp.float32))).astype(jnp.bfloat16)
    hidden_grad = jnp.dot(cotangent, weights[2].T, preferred_element_type=jnp.float32) / math.sqrt(FW)
    gate_grad = (hidden_grad * up_proj * sigmoid_gate * (1.0 + gate_pre * (1.0 - sigmoid_gate))).astype(jnp.bfloat16)
    up_grad = (hidden_grad * activated).astype(jnp.bfloat16)
    gate_delta = (jnp.dot(gate_grad.T, normed, preferred_element_type=jnp.float32) / math.sqrt(D)).astype(jnp.bfloat16)
    up_delta = (jnp.dot(up_grad.T, normed, preferred_element_type=jnp.float32) / math.sqrt(D)).astype(jnp.bfloat16)
    down_delta = (jnp.dot(hidden.T, cotangent, preferred_element_type=jnp.float32) / math.sqrt(FW)).astype(jnp.bfloat16)
    return jnp.stack([gate_delta, up_delta, down_delta])

def reference(hidden_in, teacher, params, momentum, path_alive, path_module):

    def accumulate(state_pair, which):
        summed, counts = state_pair
        module = path_module[which]
        start = (which * TOK).astype(jnp.int32)
        rows_in = lax.dynamic_slice_in_dim(hidden_in, start, TOK, 0)
        target = lax.dynamic_slice_in_dim(teacher, start, TOK, 0)
        weights = lax.dynamic_index_in_dim(params, module, 0, keepdims=False)
        pseudo_grad = path_delta(rows_in, target, weights)
        is_alive = path_alive[which].astype(jnp.float32)
        current = lax.dynamic_index_in_dim(summed, module, 0, keepdims=False)
        summed = lax.dynamic_update_index_in_dim(summed, current + is_alive * pseudo_grad.astype(jnp.float32), module, 0)
        counts = counts + is_alive * (jnp.arange(MODS, dtype=jnp.int32) == module).astype(jnp.float32)
        return ((summed, counts), None)
    initial = (jnp.zeros(params.shape, jnp.float32), jnp.zeros((MODS,), jnp.float32))
    (summed, counts), _ = lax.scan(accumulate, initial, jnp.arange(PATHS, dtype=jnp.int32))
    mean_delta = summed / counts[:, None, None, None]
    new_momentum = 0.9 * momentum + mean_delta
    new_params = (params.astype(jnp.float32) - 0.7 * (mean_delta + 0.9 * new_momentum)).astype(jnp.bfloat16)
    return (new_params, new_momentum)
```

```python
import math

import jax
import jax.numpy as jnp
from jax import lax
from jax.sharding import PartitionSpec as P

D = 2048
FW = 7168


def per_device(hidden_in, teacher, params, momentum, path_alive, path_module):
    module_count = params.shape[0]
    block_rows = params.shape[2]
    width = params.shape[3]
    path_count = path_alive.shape[0]
    contract_last = (((1,), (1,)), ((), ()))
    contract_first = (((0,), (0,)), ((), ()))
    picked = jnp.take(params, path_module, axis=0)
    rows = lax.all_to_all(picked, "path", split_axis=0, concat_axis=0, tiled=True)
    local_rows = path_count * block_rows
    rows = jnp.moveaxis(rows, 1, 0).reshape(3, local_rows, width)
    gate_rows, up_rows, down_rows = rows[0], rows[1], rows[2]
    own = hidden_in.astype(jnp.float32)
    mean_sq = jnp.mean(jnp.square(own), axis=1, keepdims=True)
    own_normed = (own * lax.rsqrt(mean_sq + 1e-05)).astype(jnp.bfloat16)
    normed = lax.all_gather(own_normed, "tensor", axis=0, tiled=True)
    gate_pre = lax.dot_general(
        normed, gate_rows, contract_last, preferred_element_type=jnp.float32
    ) / math.sqrt(D)
    up_proj = lax.dot_general(
        normed, up_rows, contract_last, preferred_element_type=jnp.float32
    ) / math.sqrt(D)
    sigmoid_gate = jax.nn.sigmoid(gate_pre)
    activated = gate_pre * sigmoid_gate
    hidden = (activated * up_proj).astype(jnp.bfloat16)
    partial_out = jnp.dot(hidden, down_rows, preferred_element_type=jnp.float32) / math.sqrt(FW)
    out_rows = lax.psum_scatter(partial_out, "tensor", scatter_dimension=0, tiled=True)
    own_count = out_rows.shape[0]
    start = lax.axis_index("tensor") * own_count
    target = lax.dynamic_slice_in_dim(teacher, start, own_count, 0)
    own_cot = (4.0 * (out_rows - target.astype(jnp.float32))).astype(jnp.bfloat16)
    cotangent = lax.all_gather(own_cot, "tensor", axis=0, tiled=True)
    down_delta = (
        lax.dot_general(hidden, cotangent, contract_first, preferred_element_type=jnp.float32)
        / math.sqrt(FW)
    ).astype(jnp.bfloat16)
    hidden_grad = lax.dot_general(
        cotangent, down_rows, contract_last, preferred_element_type=jnp.float32
    ) / math.sqrt(FW)
    gate_grad = (
        hidden_grad * up_proj * sigmoid_gate * (1.0 + gate_pre * (1.0 - sigmoid_gate))
    ).astype(jnp.bfloat16)
    up_grad = (hidden_grad * activated).astype(jnp.bfloat16)
    gate_delta = (
        lax.dot_general(gate_grad, normed, contract_first, preferred_element_type=jnp.float32)
        / math.sqrt(D)
    ).astype(jnp.bfloat16)
    up_delta = (
        lax.dot_general(up_grad, normed, contract_first, preferred_element_type=jnp.float32)
        / math.sqrt(D)
    ).astype(jnp.bfloat16)
    member = (path_module[:, None] == jnp.arange(module_count, dtype=jnp.int32)[None, :]).astype(
        jnp.int32
    ) * path_alive[:, None]
    weighting = member.astype(jnp.bfloat16)
    counts = jnp.sum(member, axis=0).astype(jnp.float32)
    deltas = jnp.stack([gate_delta, up_delta, down_delta]).reshape(3, path_count, block_rows, width)
    got = lax.all_to_all(
        jnp.moveaxis(deltas, 1, 0), "path", split_axis=0, concat_axis=0, tiled=True
    )
    summed = lax.dot_general(
        weighting, got.reshape(path_count, -1), contract_first, preferred_element_type=jnp.float32
    )
    summed = summed.reshape(module_count, 3, block_rows, width)
    mean_delta = summed / counts[:, None, None, None]
    new_momentum = 0.9 * momentum + mean_delta
    new_params = (params.astype(jnp.float32) - 0.7 * (mean_delta + 0.9 * new_momentum)).astype(
        jnp.bfloat16
    )
    return (new_params, new_momentum)


def solution(mesh):
    return jax.shard_map(
        per_device,
        mesh=mesh,
        in_specs=(
            P(("path", "tensor"), None),
            P("path", None),
            P(None, None, ("tensor", "path"), None),
            P(None, None, ("tensor", "path"), None),
            P(),
            P(),
        ),
        out_specs=(
            P(None, None, ("tensor", "path"), None),
            P(None, None, ("tensor", "path"), None),
        ),
        check_vma=False,
    )
```

```python
import math

import jax
import jax.numpy as jnp
from jax import lax
from jax.sharding import PartitionSpec as P

D = 2048
FW = 7168


def module_sums(weighting, received):
    flat = received.reshape(received.shape[0], -1)
    return lax.dot_general(
        weighting, flat, (((0,), (0,)), ((), ())), preferred_element_type=jnp.float32
    )


def ring_gather(x, axis, size):
    fwd = [(i, (i + 1) % size) for i in range(size)]
    bwd = [(i, (i - 1) % size) for i in range(size)]
    parts = [None] * size
    parts[0] = x
    ahead = x
    behind = x
    for k in range(1, size // 2 + 1):
        ahead = lax.ppermute(ahead, axis, fwd)
        parts[k] = ahead
        if k < size - k:
            behind = lax.ppermute(behind, axis, bwd)
            parts[size - k] = behind
    rev = jnp.stack([parts[(-k) % size] for k in range(size)])
    ordered = jnp.roll(rev, lax.axis_index(axis), axis=0)
    return ordered.reshape(size * x.shape[0], x.shape[1])


def per_device(hidden_in, teacher, params, momentum, path_alive, path_module):
    module_count = params.shape[0]
    block_rows = params.shape[2]
    width = params.shape[3]
    path_count = path_alive.shape[0]
    contract_last = (((1,), (1,)), ((), ()))
    contract_first = (((0,), (0,)), ((), ()))
    gate_pick = jnp.take(params[:, 0], path_module, axis=0)
    up_pick = jnp.take(params[:, 1], path_module, axis=0)
    down_pick = jnp.take(params[:, 2], path_module, axis=0)
    gate_rows, up_rows, down_rows = (
        lax.all_to_all(gate_pick, "path", split_axis=0, concat_axis=0, tiled=True),
        lax.all_to_all(up_pick, "path", split_axis=0, concat_axis=0, tiled=True),
        lax.all_to_all(down_pick, "path", split_axis=0, concat_axis=0, tiled=True),
    )
    local_rows = path_count * block_rows
    gate_rows = gate_rows.reshape(local_rows, width)
    up_rows = up_rows.reshape(local_rows, width)
    down_rows = down_rows.reshape(local_rows, width)
    own = hidden_in.astype(jnp.float32)
    mean_sq = jnp.mean(jnp.square(own), axis=1, keepdims=True)
    own_normed = (own * lax.rsqrt(mean_sq + 1e-05)).astype(jnp.bfloat16)
    normed = lax.all_gather(own_normed, "tensor", axis=0, tiled=True)
    gate_pre = lax.dot_general(
        normed, gate_rows, contract_last, preferred_element_type=jnp.float32
    ) / math.sqrt(D)
    up_proj = lax.dot_general(
        normed, up_rows, contract_last, preferred_element_type=jnp.float32
    ) / math.sqrt(D)
    sigmoid_gate = jax.nn.sigmoid(gate_pre)
    activated = gate_pre * sigmoid_gate
    hidden = (activated * up_proj).astype(jnp.bfloat16)
    partial_out = jnp.dot(hidden, down_rows, preferred_element_type=jnp.float32) / math.sqrt(FW)
    out_rows = lax.psum_scatter(partial_out, "tensor", scatter_dimension=0, tiled=True)
    own_count = out_rows.shape[0]
    start = lax.axis_index("tensor") * own_count
    target = lax.dynamic_slice_in_dim(teacher, start, own_count, 0)
    own_cot = (4.0 * (out_rows - target.astype(jnp.float32))).astype(jnp.bfloat16)
    cotangent = ring_gather(own_cot, "tensor", teacher.shape[0] // own_count)
    down_delta = (
        lax.dot_general(hidden, cotangent, contract_first, preferred_element_type=jnp.float32)
        / math.sqrt(FW)
    ).astype(jnp.bfloat16)
    hidden_grad = lax.dot_general(
        cotangent, down_rows, contract_last, preferred_element_type=jnp.float32
    ) / math.sqrt(FW)
    gate_grad = (
        hidden_grad * up_proj * sigmoid_gate * (1.0 + gate_pre * (1.0 - sigmoid_gate))
    ).astype(jnp.bfloat16)
    up_grad = (hidden_grad * activated).astype(jnp.bfloat16)
    member = (path_module[:, None] == jnp.arange(module_count, dtype=jnp.int32)[None, :]).astype(
        jnp.int32
    ) * path_alive[:, None]
    weighting = member.astype(jnp.bfloat16)
    counts = jnp.sum(member, axis=0).astype(jnp.float32)
    piece_shape = (path_count, block_rows, width)
    gate_delta = (
        lax.dot_general(gate_grad, normed, contract_first, preferred_element_type=jnp.float32)
        / math.sqrt(D)
    ).astype(jnp.bfloat16)
    up_delta = (
        lax.dot_general(up_grad, normed, contract_first, preferred_element_type=jnp.float32)
        / math.sqrt(D)
    ).astype(jnp.bfloat16)
    gate_got, up_got, down_got = (
        lax.all_to_all(
            gate_delta.reshape(piece_shape), "path", split_axis=0, concat_axis=0, tiled=True
        ),
        lax.all_to_all(
            up_delta.reshape(piece_shape), "path", split_axis=0, concat_axis=0, tiled=True
        ),
        lax.all_to_all(
            down_delta.reshape(piece_shape), "path", split_axis=0, concat_axis=0, tiled=True
        ),
    )
    summed = jnp.stack(
        [
            module_sums(weighting, gate_got),
            module_sums(weighting, up_got),
            module_sums(weighting, down_got),
        ],
        axis=1,
    )
    summed = summed.reshape(module_count, 3, block_rows, width)
    mean_delta = summed / counts[:, None, None, None]
    new_momentum = 0.9 * momentum + mean_delta
    new_params = (params.astype(jnp.float32) - 0.7 * (mean_delta + 0.9 * new_momentum)).astype(
        jnp.bfloat16
    )
    return (new_params, new_momentum)


def solution(mesh):
    return jax.shard_map(
        per_device,
        mesh=mesh,
        in_specs=(
            P(("path", "tensor"), None),
            P("path", None),
            P(None, None, ("tensor", "path"), None),
            P(None, None, ("tensor", "path"), None),
            P(),
            P(),
        ),
        out_specs=(
            P(None, None, ("tensor", "path"), None),
            P(None, None, ("tensor", "path"), None),
        ),
        check_vma=False,
    )
```

```python
import math

import jax
import jax.numpy as jnp
from jax import lax
from jax.sharding import PartitionSpec as P

D = 2048
FW = 7168


def per_device(hidden_in, teacher, params, momentum, path_alive, path_module):
    module_count = params.shape[0]
    block_rows = params.shape[2]
    width = params.shape[3]
    path_count = path_alive.shape[0]
    picked = jnp.take(params, path_module, axis=0)
    rows = lax.all_to_all(picked, "path", split_axis=0, concat_axis=0, tiled=True)
    own = hidden_in.astype(jnp.float32)
    mean_sq = jnp.mean(jnp.square(own), axis=1, keepdims=True)
    own_normed = (own * lax.rsqrt(mean_sq + 1e-05)).astype(jnp.bfloat16)
    normed = lax.all_gather(own_normed, "tensor", axis=0, tiled=True)
    proj = lax.dot_general(
        normed, rows, (((1,), (3,)), ((), ())), preferred_element_type=jnp.float32
    ) / math.sqrt(D)
    gate_pre = proj[:, :, 0, :]
    up_proj = proj[:, :, 1, :]
    down_rows = rows[:, 2]
    sigmoid_gate = jax.nn.sigmoid(gate_pre)
    activated = gate_pre * sigmoid_gate
    hidden = (activated * up_proj).astype(jnp.bfloat16)
    partial_out = lax.dot_general(
        hidden, down_rows, (((1, 2), (0, 1)), ((), ())), preferred_element_type=jnp.float32
    ) / math.sqrt(FW)
    output = lax.psum(partial_out, "tensor")
    cotangent = (4.0 * (output - teacher.astype(jnp.float32))).astype(jnp.bfloat16)
    down_delta = (
        lax.dot_general(hidden, cotangent, (((0,), (0,)), ((), ())), preferred_element_type=jnp.float32)
        / math.sqrt(FW)
    ).astype(jnp.bfloat16)
    down_got = lax.all_to_all(down_delta, "path", split_axis=0, concat_axis=0, tiled=True)
    hidden_grad = lax.dot_general(
        cotangent, down_rows, (((1,), (2,)), ((), ())), preferred_element_type=jnp.float32
    ) / math.sqrt(FW)
    gate_grad = (
        hidden_grad * up_proj * sigmoid_gate * (1.0 + gate_pre * (1.0 - sigmoid_gate))
    ).astype(jnp.bfloat16)
    up_grad = (hidden_grad * activated).astype(jnp.bfloat16)
    grads = jnp.stack([gate_grad, up_grad], axis=2)
    gu_delta = (
        lax.dot_general(grads, normed, (((0,), (0,)), ((), ())), preferred_element_type=jnp.float32)
        / math.sqrt(D)
    ).astype(jnp.bfloat16)
    gu_got = lax.all_to_all(gu_delta, "path", split_axis=0, concat_axis=0, tiled=True)
    member = (path_module[:, None] == jnp.arange(module_count, dtype=jnp.int32)[None, :]).astype(
        jnp.int32
    ) * path_alive[:, None]
    weighting = member.astype(jnp.bfloat16)
    counts = jnp.sum(member, axis=0).astype(jnp.float32)
    contract_first = (((0,), (0,)), ((), ()))
    down_sum = lax.dot_general(
        weighting, down_got.reshape(path_count, -1), contract_first, preferred_element_type=jnp.float32
    ).reshape(module_count, 1, block_rows, width)
    gu_sum = lax.dot_general(
        weighting, gu_got.reshape(path_count, -1), contract_first, preferred_element_type=jnp.float32
    ).reshape(module_count, 2, block_rows, width)
    summed = jnp.concatenate([gu_sum, down_sum], axis=1)
    mean_delta = summed / counts[:, None, None, None]
    new_momentum = 0.9 * momentum + mean_delta
    new_params = (params.astype(jnp.float32) - 0.7 * (mean_delta + 0.9 * new_momentum)).astype(
        jnp.bfloat16
    )
    return (new_params, new_momentum)


def solution(mesh):
    return jax.shard_map(
        per_device,
        mesh=mesh,
        in_specs=(
            P(("path", "tensor"), None),
            P("path", None),
            P(None, None, ("tensor", "path"), None),
            P(None, None, ("tensor", "path"), None),
            P(),
            P(),
        ),
        out_specs=(
            P(None, None, ("tensor", "path"), None),
            P(None, None, ("tensor", "path"), None),
        ),
        check_vma=False,
    )
```

```python
import math

import jax
import jax.numpy as jnp
from jax import lax
from jax.sharding import PartitionSpec as P

D = 2048
FW = 7168


def per_device(hidden_in, teacher, params, momentum, path_alive, path_module):
    module_count = params.shape[0]
    block_rows = params.shape[2]
    width = params.shape[3]
    path_count = path_alive.shape[0]
    contract_last = (((1,), (1,)), ((), ()))
    contract_first = (((0,), (0,)), ((), ()))
    picked = jnp.transpose(jnp.take(params, path_module, axis=0), (1, 2, 0, 3))
    rows = lax.all_to_all(picked, "path", split_axis=2, concat_axis=2, tiled=True)
    local_rows = path_count * block_rows
    rows = rows.reshape(3, local_rows, width)
    gate_rows, up_rows, down_rows = rows[0], rows[1], rows[2]
    own = hidden_in.astype(jnp.float32)
    mean_sq = jnp.mean(jnp.square(own), axis=1, keepdims=True)
    own_normed = (own * lax.rsqrt(mean_sq + 1e-05)).astype(jnp.bfloat16)
    normed = lax.all_gather(own_normed, "tensor", axis=0, tiled=True)
    gate_pre = lax.dot_general(
        normed, gate_rows, contract_last, preferred_element_type=jnp.float32
    ) / math.sqrt(D)
    up_proj = lax.dot_general(
        normed, up_rows, contract_last, preferred_element_type=jnp.float32
    ) / math.sqrt(D)
    sigmoid_gate = jax.nn.sigmoid(gate_pre)
    activated = gate_pre * sigmoid_gate
    hidden = (activated * up_proj).astype(jnp.bfloat16)
    partial_out = jnp.dot(hidden, down_rows, preferred_element_type=jnp.float32) / math.sqrt(FW)
    output = lax.psum(partial_out, "tensor")
    cotangent = (4.0 * (output - teacher.astype(jnp.float32))).astype(jnp.bfloat16)
    piece_shape = (block_rows, path_count, width)

    def send_back(delta):
        return lax.all_to_all(
            delta.reshape(piece_shape), "path", split_axis=1, concat_axis=1, tiled=True
        )

    down_delta = (
        lax.dot_general(hidden, cotangent, contract_first, preferred_element_type=jnp.float32)
        / math.sqrt(FW)
    ).astype(jnp.bfloat16)
    down_got = send_back(down_delta)
    hidden_grad = lax.dot_general(
        cotangent, down_rows, contract_last, preferred_element_type=jnp.float32
    ) / math.sqrt(FW)
    gate_grad = (
        hidden_grad * up_proj * sigmoid_gate * (1.0 + gate_pre * (1.0 - sigmoid_gate))
    ).astype(jnp.bfloat16)
    up_grad = (hidden_grad * activated).astype(jnp.bfloat16)
    gate_delta = (
        lax.dot_general(gate_grad, normed, contract_first, preferred_element_type=jnp.float32)
        / math.sqrt(D)
    ).astype(jnp.bfloat16)
    gate_got = send_back(gate_delta)
    up_delta = (
        lax.dot_general(up_grad, normed, contract_first, preferred_element_type=jnp.float32)
        / math.sqrt(D)
    ).astype(jnp.bfloat16)
    up_got = send_back(up_delta)
    member = (path_module[:, None] == jnp.arange(module_count, dtype=jnp.int32)[None, :]).astype(
        jnp.int32
    ) * path_alive[:, None]
    counts = jnp.sum(member, axis=0).astype(jnp.float32)
    weights_t = member.T.astype(jnp.float32)

    def module_sums(got):
        return jnp.sum(got.astype(jnp.float32)[None] * weights_t[:, None, :, None], axis=2)

    summed = jnp.stack([module_sums(gate_got), module_sums(up_got), module_sums(down_got)], axis=1)
    mean_delta = summed / counts[:, None, None, None]
    new_momentum = 0.9 * momentum + mean_delta
    new_params = (params.astype(jnp.float32) - 0.7 * (mean_delta + 0.9 * new_momentum)).astype(
        jnp.bfloat16
    )
    return (new_params, new_momentum)


def solution(mesh):
    return jax.shard_map(
        per_device,
        mesh=mesh,
        in_specs=(
            P(("path", "tensor"), None),
            P("path", None),
            P(None, None, ("tensor", "path"), None),
            P(None, None, ("tensor", "path"), None),
            P(),
            P(),
        ),
        out_specs=(
            P(None, None, ("tensor", "path"), None),
            P(None, None, ("tensor", "path"), None),
        ),
        check_vma=False,
    )
```

```python
import math

import jax
import jax.numpy as jnp
from jax import lax
from jax.sharding import PartitionSpec as P

D = 2048
FW = 7168


def per_device(hidden_in, teacher, params, momentum, path_alive, path_module):
    module_count = params.shape[0]
    block_rows = params.shape[2]
    width = params.shape[3]
    path_count = path_alive.shape[0]
    contract_last = (((1,), (1,)), ((), ()))
    contract_first = (((0,), (0,)), ((), ()))
    picked = jnp.transpose(jnp.take(params, path_module, axis=0, mode="clip"), (1, 2, 0, 3))
    rows = lax.all_to_all(picked, "path", split_axis=2, concat_axis=2, tiled=True)
    local_rows = path_count * block_rows
    rows = rows.reshape(3, local_rows, width)
    gate_rows, up_rows, down_rows = rows[0], rows[1], rows[2]
    own = hidden_in.astype(jnp.float32)
    mean_sq = jnp.mean(jnp.square(own), axis=1, keepdims=True)
    own_normed = (own * lax.rsqrt(mean_sq + 1e-05)).astype(jnp.bfloat16)
    normed = lax.all_gather(own_normed, "tensor", axis=0, tiled=True)
    gate_pre = lax.dot_general(
        normed, gate_rows, contract_last, preferred_element_type=jnp.float32
    ) / math.sqrt(D)
    up_proj = lax.dot_general(
        normed, up_rows, contract_last, preferred_element_type=jnp.float32
    ) / math.sqrt(D)
    sigmoid_gate = jax.nn.sigmoid(gate_pre)
    activated = gate_pre * sigmoid_gate
    hidden = (activated * up_proj).astype(jnp.bfloat16)
    partial_out = jnp.dot(hidden, down_rows, preferred_element_type=jnp.float32) / math.sqrt(FW)
    output = lax.psum(partial_out, "tensor")
    cotangent = (4.0 * (output - teacher.astype(jnp.float32))).astype(jnp.bfloat16)
    piece_shape = (block_rows, path_count, width)

    def send_back(delta):
        return lax.all_to_all(
            delta.reshape(piece_shape), "path", split_axis=1, concat_axis=1, tiled=True
        )

    down_delta = (
        lax.dot_general(hidden, cotangent, contract_first, preferred_element_type=jnp.float32)
        / math.sqrt(FW)
    ).astype(jnp.bfloat16)
    down_got = send_back(down_delta)
    hidden_grad = lax.dot_general(
        cotangent, down_rows, contract_last, preferred_element_type=jnp.float32
    ) / math.sqrt(FW)
    gate_grad = (
        hidden_grad * up_proj * sigmoid_gate * (1.0 + gate_pre * (1.0 - sigmoid_gate))
    ).astype(jnp.bfloat16)
    up_grad = (hidden_grad * activated).astype(jnp.bfloat16)
    gate_delta = (
        lax.dot_general(gate_grad, normed, contract_first, preferred_element_type=jnp.float32)
        / math.sqrt(D)
    ).astype(jnp.bfloat16)
    gate_got = send_back(gate_delta)
    up_delta = (
        lax.dot_general(up_grad, normed, contract_first, preferred_element_type=jnp.float32)
        / math.sqrt(D)
    ).astype(jnp.bfloat16)
    up_got = send_back(up_delta)
    member = (path_module[:, None] == jnp.arange(module_count, dtype=jnp.int32)[None, :]).astype(
        jnp.int32
    ) * path_alive[:, None]
    counts = jnp.sum(member, axis=0).astype(jnp.float32)
    new_momentum = []
    new_params = []
    weighting = member.astype(jnp.bfloat16)
    for j, got in enumerate((gate_got, up_got, down_got)):
        got, weighting_j, momentum_j, params_j = lax.optimization_barrier(
            (got, weighting, momentum[:, j], params[:, j])
        )
        summed = lax.dot_general(
            weighting_j, got, (((0,), (1,)), ((), ())), preferred_element_type=jnp.float32
        )
        mean_delta = summed / counts[:, None, None]
        momentum_j = 0.9 * momentum_j + mean_delta
        params_j = (params_j.astype(jnp.float32) - 0.7 * (mean_delta + 0.9 * momentum_j)).astype(
            jnp.bfloat16
        )
        new_momentum.append(momentum_j)
        new_params.append(params_j)
    new_momentum = jnp.stack(new_momentum, axis=1)
    new_params = jnp.stack(new_params, axis=1)
    return (new_params, new_momentum)


def solution(mesh):
    return jax.shard_map(
        per_device,
        mesh=mesh,
        in_specs=(
            P(("path", "tensor"), None),
            P("path", None),
            P(None, None, ("tensor", "path"), None),
            P(None, None, ("tensor", "path"), None),
            P(),
            P(),
        ),
        out_specs=(
            P(None, None, ("tensor", "path"), None),
            P(None, None, ("tensor", "path"), None),
        ),
        check_vma=False,
    )
```

```python
import math

import jax
import jax.numpy as jnp
from jax import lax
from jax.sharding import PartitionSpec as P


D = 2048
FW = 7168


def per_device(hidden_in, teacher, params, momentum, path_alive, path_module):
    module_count = params.shape[0]
    block_rows = params.shape[2]
    width = params.shape[3]
    path_count = path_alive.shape[0]
    contract_last = (((1,), (1,)), ((), ()))
    contract_first = (((0,), (0,)), ((), ()))
    picked = jnp.transpose(jnp.take(params, path_module, axis=0, mode="clip"), (1, 2, 0, 3))
    rows = lax.all_to_all(picked, "path", split_axis=2, concat_axis=2, tiled=True)
    local_rows = path_count * block_rows
    rows = rows.reshape(3, local_rows, width)
    gate_rows, up_rows, down_rows = rows[0], rows[1], rows[2]
    own = hidden_in.astype(jnp.float32)
    mean_sq = jnp.mean(jnp.square(own), axis=1, keepdims=True)
    own_normed = (own * lax.rsqrt(mean_sq + 1e-05)).astype(jnp.bfloat16)
    normed = lax.all_gather(own_normed, "tensor", axis=0, tiled=True)
    gate_pre = lax.dot_general(
        normed, gate_rows, contract_last, preferred_element_type=jnp.float32
    ) / math.sqrt(D)
    up_proj = lax.dot_general(
        normed, up_rows, contract_last, preferred_element_type=jnp.float32
    ) / math.sqrt(D)
    sigmoid_gate = jax.nn.sigmoid(gate_pre)
    activated = gate_pre * sigmoid_gate
    hidden = (activated * up_proj).astype(jnp.bfloat16)
    partial_out = jnp.dot(hidden, down_rows, preferred_element_type=jnp.float32) / math.sqrt(FW)
    output = lax.psum(partial_out, "tensor")
    cotangent = (4.0 * (output - teacher.astype(jnp.float32))).astype(jnp.bfloat16)
    piece_shape = (block_rows, path_count, width)

    def send_back(delta):
        return lax.all_to_all(
            delta.reshape(piece_shape), "path", split_axis=1, concat_axis=1, tiled=True
        )

    down_delta = (
        lax.dot_general(hidden, cotangent, contract_first, preferred_element_type=jnp.float32)
        / math.sqrt(FW)
    ).astype(jnp.bfloat16)
    down_got = send_back(down_delta)
    hidden_grad = lax.dot_general(
        cotangent, down_rows, contract_last, preferred_element_type=jnp.float32
    ) / math.sqrt(FW)
    gate_grad = (
        hidden_grad * up_proj * sigmoid_gate * (1.0 + gate_pre * (1.0 - sigmoid_gate))
    ).astype(jnp.bfloat16)
    up_grad = (hidden_grad * activated).astype(jnp.bfloat16)
    gate_delta = (
        lax.dot_general(gate_grad, normed, contract_first, preferred_element_type=jnp.float32)
        / math.sqrt(D)
    ).astype(jnp.bfloat16)
    gate_got = send_back(gate_delta)
    up_delta = (
        lax.dot_general(up_grad, normed, contract_first, preferred_element_type=jnp.float32)
        / math.sqrt(D)
    ).astype(jnp.bfloat16)
    up_got = send_back(up_delta)
    member = (path_module[:, None] == jnp.arange(module_count, dtype=jnp.int32)[None, :]).astype(
        jnp.int32
    ) * path_alive[:, None]
    counts = jnp.sum(member, axis=0).astype(jnp.float32)
    new_momentum = []
    new_params = []
    weighting = member.astype(jnp.bfloat16)
    for j, got in enumerate((gate_got, up_got, down_got)):
        got, weighting_j, momentum_j, params_j, counts_j = lax.optimization_barrier(
            (got, weighting, momentum[:, j], params[:, j], counts)
        )
        summed = lax.dot_general(
            weighting_j, got, (((0,), (1,)), ((), ())), preferred_element_type=jnp.float32
        )
        mean_delta = summed / counts_j[:, None, None]
        momentum_j = 0.9 * momentum_j + mean_delta
        params_j = (params_j.astype(jnp.float32) - 0.7 * (mean_delta + 0.9 * momentum_j)).astype(
            jnp.bfloat16
        )
        new_momentum.append(momentum_j)
        new_params.append(params_j)
    new_momentum = jnp.stack(new_momentum, axis=1)
    new_params = jnp.stack(new_params, axis=1)
    return (new_params, new_momentum)


def solution(mesh):
    return jax.shard_map(
        per_device,
        mesh=mesh,
        in_specs=(
            P(("path", "tensor"), None),
            P("path", None),
            P(None, None, ("tensor", "path"), None),
            P(None, None, ("tensor", "path"), None),
            P(),
            P(),
        ),
        out_specs=(
            P(None, None, ("tensor", "path"), None),
            P(None, None, ("tensor", "path"), None),
        ),
        check_vma=False,
    )
```

```python
import math

import jax
import jax.numpy as jnp
from jax import lax
from jax.sharding import PartitionSpec as P


D = 2048
FW = 7168


def per_device(hidden_in, teacher, params, momentum, path_alive, path_module):
    module_count = params.shape[0]
    block_rows = params.shape[2]
    width = params.shape[3]
    path_count = path_alive.shape[0]
    contract_last = (((1,), (1,)), ((), ()))
    contract_first = (((0,), (0,)), ((), ()))
    picked = jnp.transpose(jnp.take(params, path_module, axis=0, mode="clip"), (1, 2, 0, 3))
    rows = lax.all_to_all(picked, "path", split_axis=2, concat_axis=2, tiled=True)
    local_rows = path_count * block_rows
    rows = rows.reshape(3, local_rows, width)
    gate_rows, up_rows, down_rows = rows[0], rows[1], rows[2]
    own = hidden_in.astype(jnp.float32)
    mean_sq = jnp.mean(jnp.square(own), axis=1, keepdims=True)
    own_normed = (own * lax.rsqrt(mean_sq + 1e-05)).astype(jnp.bfloat16)
    normed = lax.all_gather(own_normed, "tensor", axis=0, tiled=True)
    gate_pre = lax.dot_general(
        normed, gate_rows, contract_last, preferred_element_type=jnp.float32
    ) / math.sqrt(D)
    up_proj = lax.dot_general(
        normed, up_rows, contract_last, preferred_element_type=jnp.float32
    ) / math.sqrt(D)
    sigmoid_gate = jax.nn.sigmoid(gate_pre)
    activated = gate_pre * sigmoid_gate
    hidden = (activated * up_proj).astype(jnp.bfloat16)
    partial_out = jnp.dot(hidden, down_rows, preferred_element_type=jnp.float32) / math.sqrt(FW)
    output = lax.psum(partial_out, "tensor")
    cotangent = (4.0 * (output - teacher.astype(jnp.float32))).astype(jnp.bfloat16)
    piece_shape = (block_rows, path_count, width)

    def send_back(delta):
        return lax.all_to_all(
            delta.reshape(piece_shape), "path", split_axis=1, concat_axis=1, tiled=True
        )

    down_delta = (
        lax.dot_general(hidden, cotangent, contract_first, preferred_element_type=jnp.float32)
        / math.sqrt(FW)
    ).astype(jnp.bfloat16)
    down_got = send_back(down_delta)
    hidden_grad = lax.dot_general(
        cotangent, down_rows, contract_last, preferred_element_type=jnp.float32
    ) / math.sqrt(FW)
    gate_grad = (
        hidden_grad * up_proj * sigmoid_gate * (1.0 + gate_pre * (1.0 - sigmoid_gate))
    ).astype(jnp.bfloat16)
    up_grad = (hidden_grad * activated).astype(jnp.bfloat16)
    gate_delta = (
        lax.dot_general(gate_grad, normed, contract_first, preferred_element_type=jnp.float32)
        / math.sqrt(D)
    ).astype(jnp.bfloat16)
    gate_got = send_back(gate_delta)
    up_delta = (
        lax.dot_general(up_grad, normed, contract_first, preferred_element_type=jnp.float32)
        / math.sqrt(D)
    ).astype(jnp.bfloat16)
    split = block_rows - block_rows // 3
    up_pieces = up_delta.reshape(piece_shape)

    def send_rows(piece):
        return lax.all_to_all(piece, "path", split_axis=1, concat_axis=1, tiled=True)

    up_got_a = send_rows(up_pieces[:split])
    up_got_b = send_rows(up_pieces[split:])
    member = (path_module[:, None] == jnp.arange(module_count, dtype=jnp.int32)[None, :]).astype(
        jnp.int32
    ) * path_alive[:, None]
    counts = jnp.sum(member, axis=0).astype(jnp.float32)
    new_momentum = []
    new_params = []
    weighting = member.astype(jnp.bfloat16)
    parts = (
        (gate_got, 0, slice(None)),
        (up_got_a, 1, slice(0, split)),
        (up_got_b, 1, slice(split, None)),
        (down_got, 2, slice(None)),
    )
    for got, j, rows in parts:
        got, weighting_j, momentum_j, params_j, counts_j = lax.optimization_barrier(
            (got, weighting, momentum[:, j, rows], params[:, j, rows], counts)
        )
        summed = lax.dot_general(
            weighting_j, got, (((0,), (1,)), ((), ())), preferred_element_type=jnp.float32
        )
        mean_delta = summed / counts_j[:, None, None]
        momentum_j = 0.9 * momentum_j + mean_delta
        params_j = (params_j.astype(jnp.float32) - 0.7 * (mean_delta + 0.9 * momentum_j)).astype(
            jnp.bfloat16
        )
        new_momentum.append(momentum_j)
        new_params.append(params_j)
    new_momentum = [new_momentum[0], jnp.concatenate(new_momentum[1:3], axis=1), new_momentum[3]]
    new_params = [new_params[0], jnp.concatenate(new_params[1:3], axis=1), new_params[3]]
    new_momentum = jnp.stack(new_momentum, axis=1)
    new_params = jnp.stack(new_params, axis=1)
    return (new_params, new_momentum)


def solution(mesh):
    return jax.shard_map(
        per_device,
        mesh=mesh,
        in_specs=(
            P(("path", "tensor"), None),
            P("path", None),
            P(None, None, ("tensor", "path"), None),
            P(None, None, ("tensor", "path"), None),
            P(),
            P(),
        ),
        out_specs=(
            P(None, None, ("tensor", "path"), None),
            P(None, None, ("tensor", "path"), None),
        ),
        check_vma=False,
    )
```

```python
import math

import jax
import jax.numpy as jnp
from jax import lax
from jax.sharding import PartitionSpec as P


D = 2048
FW = 7168


def per_device(hidden_in, teacher, params, momentum, path_alive, path_module):
    module_count = params.shape[0]
    block_rows = params.shape[2]
    width = params.shape[3]
    path_count = path_alive.shape[0]
    contract_last = (((1,), (1,)), ((), ()))
    contract_first = (((0,), (0,)), ((), ()))
    picked = jnp.transpose(jnp.take(params, path_module, axis=0, mode="clip"), (1, 2, 0, 3))
    rows = lax.all_to_all(picked, "path", split_axis=2, concat_axis=2, tiled=True)
    local_rows = path_count * block_rows
    rows = rows.reshape(3, local_rows, width)
    gate_rows, up_rows, down_rows = rows[0], rows[1], rows[2]
    own = hidden_in.astype(jnp.float32)
    mean_sq = jnp.mean(jnp.square(own), axis=1, keepdims=True)
    own_normed = (own * lax.rsqrt(mean_sq + 1e-05)).astype(jnp.bfloat16)
    normed = lax.all_gather(own_normed, "tensor", axis=0, tiled=True)
    gate_pre = lax.dot_general(
        normed, gate_rows, contract_last, preferred_element_type=jnp.float32
    ) / math.sqrt(D)
    up_proj = lax.dot_general(
        normed, up_rows, contract_last, preferred_element_type=jnp.float32
    ) / math.sqrt(D)
    sigmoid_gate = jax.nn.sigmoid(gate_pre)
    activated = gate_pre * sigmoid_gate
    hidden = (activated * up_proj).astype(jnp.bfloat16)
    partial_out = jnp.dot(hidden, down_rows, preferred_element_type=jnp.float32) / math.sqrt(FW)
    output = lax.psum(partial_out, "tensor")
    cotangent = (4.0 * (output - teacher.astype(jnp.float32))).astype(jnp.bfloat16)
    piece_shape = (block_rows, path_count, width)

    def send_back(delta):
        return lax.all_to_all(
            delta.reshape(piece_shape), "path", split_axis=1, concat_axis=1, tiled=True
        )

    down_delta = (
        lax.dot_general(hidden, cotangent, contract_first, preferred_element_type=jnp.float32)
        / math.sqrt(FW)
    ).astype(jnp.bfloat16)
    down_got = send_back(down_delta)
    hidden_grad = lax.dot_general(
        cotangent, down_rows, contract_last, preferred_element_type=jnp.float32
    ) / math.sqrt(FW)
    gate_grad = (
        hidden_grad * up_proj * sigmoid_gate * (1.0 + gate_pre * (1.0 - sigmoid_gate))
    ).astype(jnp.bfloat16)
    up_grad = (hidden_grad * activated).astype(jnp.bfloat16)
    gate_delta = (
        lax.dot_general(gate_grad, normed, contract_first, preferred_element_type=jnp.float32)
        / math.sqrt(D)
    ).astype(jnp.bfloat16)
    gate_got = send_back(gate_delta)
    up_delta = (
        lax.dot_general(up_grad, normed, contract_first, preferred_element_type=jnp.float32)
        / math.sqrt(D)
    ).astype(jnp.bfloat16)
    up_got = send_back(up_delta)
    member = (path_module[:, None] == jnp.arange(module_count, dtype=jnp.int32)[None, :]).astype(
        jnp.int32
    ) * path_alive[:, None]
    counts = jnp.sum(member, axis=0).astype(jnp.float32)
    new_momentum = momentum
    new_params = params
    weighting = member.astype(jnp.bfloat16)
    for j, got in ((0, gate_got), (2, down_got), (1, up_got)):
        got, weighting_j, momentum_j, params_j, counts_j = lax.optimization_barrier(
            (got, weighting, momentum[:, j], params[:, j], counts)
        )
        summed = lax.dot_general(
            weighting_j, got, (((0,), (1,)), ((), ())), preferred_element_type=jnp.float32
        )
        mean_delta = summed / counts_j[:, None, None]
        momentum_j = 0.9 * momentum_j + mean_delta
        params_j = (params_j.astype(jnp.float32) - 0.7 * (mean_delta + 0.9 * momentum_j)).astype(
            jnp.bfloat16
        )
        new_momentum = new_momentum.at[:, j].set(momentum_j)
        new_params = new_params.at[:, j].set(params_j)
    return (new_params, new_momentum)


def solution(mesh):
    return jax.shard_map(
        per_device,
        mesh=mesh,
        in_specs=(
            P(("path", "tensor"), None),
            P("path", None),
            P(None, None, ("tensor", "path"), None),
            P(None, None, ("tensor", "path"), None),
            P(),
            P(),
        ),
        out_specs=(
            P(None, None, ("tensor", "path"), None),
            P(None, None, ("tensor", "path"), None),
        ),
        check_vma=False,
    )
```
